256 devices in a mesh: dp: 4 (over x), sx: 16 (over y_hi, z), sy: 4 (over y_lo, core).
Axes of the slice: x: 4, y: 4 (y_hi: 2, y_lo: 2; y = y_hi * 2 + y_lo), z: 8, core: 2. Of those that a mesh axis runs over, the one named last changes fastest.
Arguments:
- volume: bfloat16 [4, 256, 64, 32, 128], P('dp', 'sx', 'sy'), may hold values from -6 to 6
- block_active: int32 [4, 16, 4, 2], P('dp', 'sx', 'sy'), may hold values from 0 to 1, as said below
- weight: bfloat16 [3, 3, 3, 128, 128], replicated, may hold values from -0.109375 to 0.109375
- bias: float32 [128], replicated, may hold values from -3 to 3
- cotangent: bfloat16 [4, 256, 64, 32, 128], P('dp', 'sx', 'sy'), may hold values from -0.00390625 to 0.00390625
Outputs:
- activated: bfloat16 [4, 256, 64, 32, 128], P('dp', 'sx', 'sy')
- grad_weight: float32 [3, 3, 3, 128, 128], replicated
- grad_bias: float32 [128], replicated
The draws below stay inside these ranges and needn't reach their ends.
Inputs may be any that keep to these rules, and one draw needn't show every extreme that they name: `block_active`: every tile of 2 blocks along depth (one value of the first three indices) has at least one active block; the number of active blocks of a tile is drawn evenly from 1 to 2.
All inputs are finite; a program needn't handle non-finite values.
Results may differ from the reference program's by a relative error of at most 0.006.
Values may be sent and summed in bfloat16 or wider, within the bound.
No kernel may reach another device: no remote copies, remote signals or barrier semaphores. Data moves between devices by JAX's collectives and lax.ppermute only.
A program may use at most 64 MiB of HBM per device.

```python
import jax
import jax.numpy as jnp
from jax import lax

C = 128
BLK = 16
TB = 2
CROPS = 4
NBX = 16
NBY = 4
NX = 256
NY = 64
NZ = 32


def draw_block_active(key, part):
    key_count, key_order = jax.random.split(key)
    counts = jax.random.randint(key_count, (CROPS, NBX, NBY, 1), 1, TB + 1)
    scores = jax.random.randint(key_order, (CROPS, NBX, NBY, TB), 0, 1 << 20) * TB + jnp.arange(TB, dtype=jnp.int32)
    ranks = jnp.argsort(jnp.argsort(scores, axis=-1), axis=-1)
    return (ranks < counts).astype(jnp.int32)


def shard_levels(own_key, dims, shards, least, top_value):
    gain = 1.0
    for axis_at, shards_of in shards:
        heights = jax.random.uniform(jax.random.fold_in(jax.random.fold_in(own_key, 6), axis_at), (shards_of,), jnp.float32, least / len(shards), top_value / len(shards))
        gain = gain * jnp.repeat(jnp.exp(heights), dims[axis_at] // shards_of).reshape((-1,) + (1,) * (len(dims) - 1 - axis_at))
    return gain


def centred(own_key, extent, width, most, cuts=(), kind=jnp.bfloat16):
    entries = jax.random.normal(own_key, extent, jnp.float32) * width
    if len(cuts) > 0:
        entries = shard_levels(own_key, extent, cuts, -0.22, 0.18) * entries
    return jnp.clip(entries, min=-most, max=most).astype(kind)


def setup_inputs(seed: int = 0) -> dict:
    key_list = jax.random.split(jax.random.key(seed), 6)
    return {
        "volume": centred(key_list[0], (CROPS, NX, NY, NZ, C), 1.0, 6.0, ((0, 4), (1, 16), (2, 4))),
        "block_active": draw_block_active(jax.random.fold_in(key_list[5], 71), 0),
        "weight": centred(key_list[2], (3, 3, 3, C, C), (27 * C) ** -0.5, 0.109375),
        "bias": centred(key_list[3], (C,), 0.5, 3.0, (), jnp.float32),
        "cotangent": centred(key_list[4], (CROPS, NX, NY, NZ, C), (CROPS * NX * NY * NZ) ** -0.5, 0.00390625, ((0, 4), (1, 16), (2, 4))),
    }


def reference(volume, block_active, weight, bias, cotangent):
    kernel = weight.astype(jnp.float32)

    def one_crop(items):
        vol, act, cot = items
        vox = jnp.repeat(jnp.repeat(jnp.repeat(act, BLK, 0), BLK, 1), BLK, 2).astype(jnp.float32)[..., None]
        masked = (vol.astype(jnp.float32) * vox)[None]
        padded = jnp.pad(masked, ((0, 0), (1, 1), (1, 1), (1, 1), (0, 0)))
        pre = lax.conv_general_dilated(padded, kernel, (1, 1, 1), "VALID", dimension_numbers=("NDHWC", "DHWIO", "NDHWC"), precision=lax.Precision.HIGHEST) + bias
        sig = jax.nn.sigmoid(pre)
        out = (pre * sig * vox[None]).astype(jnp.bfloat16)
        dpre = (cot[None].astype(jnp.float32) * sig * (1.0 + pre * (1.0 - sig)) * vox[None]).astype(jnp.bfloat16)
        dpre = lax.optimization_barrier(dpre).astype(jnp.float32)
        grads = []
        for a in range(3):
            for b in range(3):
                for c in range(3):
                    piece = padded[:, a:a + NX, b:b + NY, c:c + NZ, :]
                    grads.append(lax.dot_general(piece, dpre, (((0, 1, 2, 3), (0, 1, 2, 3)), ((), ())), precision=lax.Precision.HIGHEST))
        grad_w = jnp.stack(grads).reshape(3, 3, 3, C, C)
        grad_b = jnp.sum(dpre, axis=(0, 1, 2, 3))
        return out[0], grad_w, grad_b

    outs, grad_ws, grad_bs = lax.map(one_crop, (volume, block_active, cotangent))
    return outs, jnp.sum(grad_ws, axis=0), jnp.sum(grad_bs, axis=0)
```

```python
import jax
import jax.numpy as jnp
from jax import lax
from jax.sharding import Mesh, PartitionSpec as P


def with_halo(block, sides, width):
    for axis, dim in sides:
        count = lax.axis_size(axis)
        forward = [(i, i + 1) for i in range(count - 1)]
        backward = [(target, source) for source, target in forward]
        low = lax.ppermute(
            lax.slice_in_dim(block, block.shape[dim] - width, None, axis=dim), axis, forward
        )
        high = lax.ppermute(lax.slice_in_dim(block, 0, width, axis=dim), axis, backward)
        block = jnp.concatenate([low, block, high], axis=dim)
    return block


def layer_work(slab, cot_piece, vox_mask, weight, bias):
    pre = (
        lax.conv_general_dilated(
            slab,
            weight,
            (1, 1, 1),
            "VALID",
            dimension_numbers=("NDHWC", "DHWIO", "NDHWC"),
            preferred_element_type=jnp.float32,
        )
        + bias
    )
    sig = jax.nn.sigmoid(pre)
    out = (pre * sig * vox_mask).astype(jnp.bfloat16)
    dpre = (cot_piece.astype(jnp.float32) * sig * (1.0 + pre * (1.0 - sig)) * vox_mask).astype(
        jnp.bfloat16
    )
    span_x = cot_piece.shape[1]
    span_y = cot_piece.shape[2]
    span_z = cot_piece.shape[3]
    channels = cot_piece.shape[4]
    grads = []
    for a in range(3):
        for b in range(3):
            for c in range(3):
                piece = slab[:, a : a + span_x, b : b + span_y, c : c + span_z, :]
                grads.append(
                    lax.dot_general(
                        piece,
                        dpre,
                        (((0, 1, 2, 3), (0, 1, 2, 3)), ((), ())),
                        preferred_element_type=jnp.float32,
                    )
                )
    grad_w = jnp.stack(grads).reshape(3, 3, 3, channels, channels)
    grad_b = jnp.sum(dpre.astype(jnp.float32), axis=(0, 1, 2, 3))
    return (out, grad_w, grad_b)


def group_size(axes):
    size = 1
    for axis in axes:
        size *= lax.axis_size(axis)
    return size


def scatter_sum(flat, axes):
    parts = lax.all_to_all(flat.reshape(group_size(axes), -1), axes, 0, 0, tiled=True)
    return parts.sum(0)


def gather_back(piece, axes):
    count = group_size(axes)
    parts = jnp.broadcast_to(piece[None], (count,) + piece.shape)
    return lax.all_to_all(parts, axes, 0, 0, tiled=True).reshape(-1)


STAGES = (("yh", "yl", "c"), ("x", "z"))


def reduce_grads(grad_w, grad_b):
    total = grad_w.size + grad_b.size
    devices = group_size(sum(STAGES, ()))
    padded = -(-total // devices) * devices
    flat = jnp.concatenate(
        [grad_w.reshape(-1), grad_b, jnp.zeros((padded - total,), jnp.float32)]
    )
    for axes in STAGES:
        flat = scatter_sum(flat, axes)
    for axes in reversed(STAGES):
        flat = gather_back(flat, axes)
    return flat[: grad_w.size].reshape(grad_w.shape), flat[grad_w.size : total]


def local(volume, block_active, weight, bias, cotangent):
    depth = volume.shape[3]
    blocks = block_active.shape[3]
    edge = depth // blocks
    vox_mask = jnp.repeat(block_active, edge, axis=3)[..., None].astype(jnp.float32)
    masked = volume * vox_mask.astype(jnp.bfloat16)
    padded = with_halo(masked, ((("yh", "z"), 1), (("yl", "c"), 2)), 1)
    padded = jnp.pad(padded, ((0, 0), (0, 0), (0, 0), (1, 1), (0, 0)))
    activated, grad_w, grad_b = layer_work(padded, cotangent, vox_mask, weight, bias)
    grad_w, grad_b = reduce_grads(grad_w, grad_b)
    return (activated, grad_w, grad_b)


def solution(mesh):
    dp, sx, sy = (mesh.shape[name] for name in ("dp", "sx", "sy"))
    shape = (dp, 2, sx // 2, sy // 2, 2)
    physical = Mesh(mesh.devices.reshape(shape), ("x", "yh", "z", "yl", "c"))
    tiles = ("x", ("yh", "z"), ("yl", "c"))
    placed = (
        P(*tiles, None, None),
        P(*tiles, None),
        P(),
        P(),
        P(*tiles, None, None),
    )
    return jax.shard_map(
        local,
        mesh=physical,
        in_specs=placed,
        out_specs=(P(*tiles, None, None), P(), P()),
        check_vma=False,
    )
```

```python
import jax
import jax.numpy as jnp
from jax import lax
from jax.sharding import Mesh, PartitionSpec as P


def with_halo(block, sides, width):
    for axis, dim in sides:
        count = lax.axis_size(axis)
        forward = [(i, i + 1) for i in range(count - 1)]
        backward = [(target, source) for source, target in forward]
        low = lax.ppermute(
            lax.slice_in_dim(block, block.shape[dim] - width, None, axis=dim), axis, forward
        )
        high = lax.ppermute(lax.slice_in_dim(block, 0, width, axis=dim), axis, backward)
        block = jnp.concatenate([low, block, high], axis=dim)
    return block


def layer_work(slab, cot_piece, vox_mask, weight, bias):
    pre = (
        lax.conv_general_dilated(
            slab,
            weight,
            (1, 1, 1),
            "VALID",
            dimension_numbers=("NDHWC", "DHWIO", "NDHWC"),
            preferred_element_type=jnp.float32,
        )
        + bias
    )
    sig = jax.nn.sigmoid(pre)
    out = (pre * sig * vox_mask).astype(jnp.bfloat16)
    dpre = (cot_piece.astype(jnp.float32) * sig * (1.0 + pre * (1.0 - sig)) * vox_mask).astype(
        jnp.bfloat16
    )
    span_x = cot_piece.shape[1]
    span_y = cot_piece.shape[2]
    span_z = cot_piece.shape[3]
    channels = cot_piece.shape[4]
    grads = []
    for a in range(3):
        for b in range(3):
            for c in range(3):
                piece = slab[:, a : a + span_x, b : b + span_y, c : c + span_z, :]
                grads.append(
                    lax.dot_general(
                        piece,
                        dpre,
                        (((0, 1, 2, 3), (0, 1, 2, 3)), ((), ())),
                        preferred_element_type=jnp.float32,
                    )
                )
    grad_w = jnp.stack(grads).reshape(3, 3, 3, channels, channels)
    grad_b = jnp.sum(dpre.astype(jnp.float32), axis=(0, 1, 2, 3))
    return (out, grad_w, grad_b)


def group_size(axes):
    size = 1
    for axis in axes:
        size *= lax.axis_size(axis)
    return size


def scatter_sum(flat, axes):
    parts = lax.all_to_all(flat.reshape(group_size(axes), -1), axes, 0, 0, tiled=True)
    return parts.sum(0)


def gather_back(piece, axes):
    count = group_size(axes)
    parts = jnp.broadcast_to(piece[None], (count,) + piece.shape)
    return lax.all_to_all(parts, axes, 0, 0, tiled=True).reshape(-1)


def halve_sum(flat, axis):
    upper = lax.axis_index(axis) % 2
    halves = flat.reshape(2, -1)
    keep = jnp.where(upper == 0, halves[0], halves[1])
    send = jnp.where(upper == 0, halves[1], halves[0])
    return keep + lax.ppermute(send, axis, [(0, 1), (1, 0)])


def double_back(piece, axis):
    upper = lax.axis_index(axis) % 2
    other = lax.ppermute(piece, axis, [(0, 1), (1, 0)])
    return jnp.where(
        upper == 0, jnp.concatenate([piece, other]), jnp.concatenate([other, piece])
    )


STAGES = (("yh", "yl"), ("x", "z"))


def reduce_grads(grad_w, grad_b):
    total = grad_w.size + grad_b.size
    devices = 2 * group_size(sum(STAGES, ()))
    padded = -(-total // devices) * devices
    flat = jnp.concatenate(
        [grad_w.reshape(-1), grad_b, jnp.zeros((padded - total,), jnp.float32)]
    )
    flat = halve_sum(flat, "c")
    for axes in STAGES:
        flat = scatter_sum(flat, axes)
    for axes in reversed(STAGES):
        flat = gather_back(flat, axes)
    flat = double_back(flat, "c")
    return flat[: grad_w.size].reshape(grad_w.shape), flat[grad_w.size : total]


def local(volume, block_active, weight, bias, cotangent):
    depth = volume.shape[3]
    blocks = block_active.shape[3]
    edge = depth // blocks
    vox_mask = jnp.repeat(block_active, edge, axis=3)[..., None].astype(jnp.float32)
    masked = volume * vox_mask.astype(jnp.bfloat16)
    padded = with_halo(masked, ((("yh", "z"), 1), (("yl", "c"), 2)), 1)
    padded = jnp.pad(padded, ((0, 0), (0, 0), (0, 0), (1, 1), (0, 0)))
    activated, grad_w, grad_b = layer_work(padded, cotangent, vox_mask, weight, bias)
    grad_w, grad_b = reduce_grads(grad_w, grad_b)
    return (activated, grad_w, grad_b)


def solution(mesh):
    dp, sx, sy = (mesh.shape[name] for name in ("dp", "sx", "sy"))
    shape = (dp, 2, sx // 2, sy // 2, 2)
    physical = Mesh(mesh.devices.reshape(shape), ("x", "yh", "z", "yl", "c"))
    tiles = ("x", ("yh", "z"), ("yl", "c"))
    placed = (
        P(*tiles, None, None),
        P(*tiles, None),
        P(),
        P(),
        P(*tiles, None, None),
    )
    return jax.shard_map(
        local,
        mesh=physical,
        in_specs=placed,
        out_specs=(P(*tiles, None, None), P(), P()),
        check_vma=False,
    )
```

```python
import jax
import jax.numpy as jnp
from jax import lax
from jax.sharding import Mesh, PartitionSpec as P


def with_halo(block, sides, width):
    for axis, dim in sides:
        count = lax.axis_size(axis)
        forward = [(i, i + 1) for i in range(count - 1)]
        backward = [(target, source) for source, target in forward]
        low = lax.ppermute(
            lax.slice_in_dim(block, block.shape[dim] - width, None, axis=dim), axis, forward
        )
        high = lax.ppermute(lax.slice_in_dim(block, 0, width, axis=dim), axis, backward)
        block = jnp.concatenate([low, block, high], axis=dim)
    return block


def layer_work(slab, cot_piece, vox_mask, weight, bias):
    pre = (
        lax.conv_general_dilated(
            slab,
            weight,
            (1, 1, 1),
            "VALID",
            dimension_numbers=("NDHWC", "DHWIO", "NDHWC"),
            preferred_element_type=jnp.float32,
        )
        + bias
    )
    sig = jax.nn.sigmoid(pre)
    out = (pre * sig * vox_mask).astype(jnp.bfloat16)
    dpre = (cot_piece.astype(jnp.float32) * sig * (1.0 + pre * (1.0 - sig)) * vox_mask).astype(
        jnp.bfloat16
    )
    span_x = cot_piece.shape[1]
    span_y = cot_piece.shape[2]
    span_z = cot_piece.shape[3]
    channels = cot_piece.shape[4]
    grads = []
    for a in range(3):
        for b in range(3):
            for c in range(3):
                piece = slab[:, a : a + span_x, b : b + span_y, c : c + span_z, :]
                grads.append(
                    lax.dot_general(
                        piece,
                        dpre,
                        (((0, 1, 2, 3), (0, 1, 2, 3)), ((), ())),
                        preferred_element_type=jnp.float32,
                    )
                )
    grad_w = jnp.stack(grads).reshape(3, 3, 3, channels, channels)
    grad_b = jnp.sum(dpre.astype(jnp.float32), axis=(0, 1, 2, 3))
    return (out, grad_w, grad_b)


def group_size(axes):
    size = 1
    for axis in axes:
        size *= lax.axis_size(axis)
    return size


def scatter_sum(flat, axes):
    parts = lax.all_to_all(flat.reshape(group_size(axes), -1), axes, 0, 0, tiled=True)
    return parts.sum(0)


def gather_back(piece, axes):
    count = group_size(axes)
    parts = jnp.broadcast_to(piece[None], (count,) + piece.shape)
    return lax.all_to_all(parts, axes, 0, 0, tiled=True).reshape(-1)


def halve_sum(flat, axis):
    upper = lax.axis_index(axis) % 2
    halves = flat.reshape(2, -1)
    keep = jnp.where(upper == 0, halves[0], halves[1])
    send = jnp.where(upper == 0, halves[1], halves[0])
    return keep + lax.ppermute(send, axis, [(0, 1), (1, 0)])


def double_back(piece, axis):
    upper = lax.axis_index(axis) % 2
    other = lax.ppermute(piece, axis, [(0, 1), (1, 0)])
    return jnp.where(
        upper == 0, jnp.concatenate([piece, other]), jnp.concatenate([other, piece])
    )


STAGES = (("yh", "yl"), ("x", "z"))


def reduce_grads(grad_w, grad_b):
    total = grad_w.size + grad_b.size
    unit = 2 * group_size(sum(STAGES, ())) * 128
    padded = -(-total // unit) * unit
    flat = jnp.concatenate(
        [grad_w.reshape(-1), grad_b, jnp.zeros((padded - total,), jnp.float32)]
    )
    flat = halve_sum(flat, "c")
    for axes in STAGES:
        flat = scatter_sum(flat, axes)
    for axes in reversed(STAGES):
        flat = gather_back(flat, axes)
    flat = double_back(flat, "c")
    return flat[: grad_w.size].reshape(grad_w.shape), flat[grad_w.size : total]


def local(volume, block_active, weight, bias, cotangent):
    depth = volume.shape[3]
    blocks = block_active.shape[3]
    edge = depth // blocks
    vox_mask = jnp.repeat(block_active, edge, axis=3)[..., None].astype(jnp.float32)
    masked = volume * vox_mask.astype(jnp.bfloat16)
    padded = with_halo(masked, ((("yh", "z"), 1), (("yl", "c"), 2)), 1)
    padded = jnp.pad(padded, ((0, 0), (0, 0), (0, 0), (1, 1), (0, 0)))
    activated, grad_w, grad_b = layer_work(padded, cotangent, vox_mask, weight, bias)
    grad_w, grad_b = reduce_grads(grad_w, grad_b)
    return (activated, grad_w, grad_b)


def solution(mesh):
    dp, sx, sy = (mesh.shape[name] for name in ("dp", "sx", "sy"))
    shape = (dp, 2, sx // 2, sy // 2, 2)
    physical = Mesh(mesh.devices.reshape(shape), ("x", "yh", "z", "yl", "c"))
    tiles = ("x", ("yh", "z"), ("yl", "c"))
    placed = (
        P(*tiles, None, None),
        P(*tiles, None),
        P(),
        P(),
        P(*tiles, None, None),
    )
    return jax.shard_map(
        local,
        mesh=physical,
        in_specs=placed,
        out_specs=(P(*tiles, None, None), P(), P()),
        check_vma=False,
    )
```

```python
import jax
import jax.numpy as jnp
from jax import lax
from jax.sharding import Mesh, PartitionSpec as P


def with_halo(block, sides, width):
    for axis, dim in sides:
        count = lax.axis_size(axis)
        forward = [(i, i + 1) for i in range(count - 1)]
        backward = [(target, source) for source, target in forward]
        low = lax.ppermute(
            lax.slice_in_dim(block, block.shape[dim] - width, None, axis=dim), axis, forward
        )
        high = lax.ppermute(lax.slice_in_dim(block, 0, width, axis=dim), axis, backward)
        block = jnp.concatenate([low, block, high], axis=dim)
    return block


def layer_work(slab, cot_piece, vox_mask, weight, bias):
    pre = (
        lax.conv_general_dilated(
            slab,
            weight,
            (1, 1, 1),
            "VALID",
            dimension_numbers=("NDHWC", "DHWIO", "NDHWC"),
            preferred_element_type=jnp.float32,
        )
        + bias
    )
    sig = jax.nn.sigmoid(pre)
    out = (pre * sig * vox_mask).astype(jnp.bfloat16)
    dpre = (cot_piece.astype(jnp.float32) * sig * (1.0 + pre * (1.0 - sig)) * vox_mask).astype(
        jnp.bfloat16
    )
    span_x = cot_piece.shape[1]
    span_y = cot_piece.shape[2]
    span_z = cot_piece.shape[3]
    channels = cot_piece.shape[4]
    grads = []
    for a in range(3):
        for b in range(3):
            for c in range(3):
                piece = slab[:, a : a + span_x, b : b + span_y, c : c + span_z, :]
                grads.append(
                    lax.dot_general(
                        piece,
                        dpre,
                        (((0, 1, 2, 3), (0, 1, 2, 3)), ((), ())),
                        preferred_element_type=jnp.float32,
                    )
                )
    grad_w = jnp.stack(grads).reshape(3, 3, 3, channels, channels)
    grad_b = jnp.sum(dpre.astype(jnp.float32), axis=(0, 1, 2, 3))
    return (out, grad_w, grad_b)


def group_size(axes):
    size = 1
    for axis in axes:
        size *= lax.axis_size(axis)
    return size


def scatter_sum(flat, axes):
    parts = lax.all_to_all(flat.reshape(group_size(axes), -1), axes, 0, 0, tiled=True)
    return parts.sum(0)


def gather_back(piece, axes):
    count = group_size(axes)
    parts = jnp.broadcast_to(piece[None], (count,) + piece.shape)
    return lax.all_to_all(parts, axes, 0, 0, tiled=True).reshape(-1)


def halve_sum(flat, axis):
    upper = lax.axis_index(axis) % 2
    halves = flat.reshape(2, -1)
    keep = jnp.where(upper == 0, halves[0], halves[1])
    send = jnp.where(upper == 0, halves[1], halves[0])
    return keep + lax.ppermute(send, axis, [(0, 1), (1, 0)])


def double_back(piece, axis):
    upper = lax.axis_index(axis) % 2
    other = lax.ppermute(piece, axis, [(0, 1), (1, 0)])
    return jnp.where(
        upper == 0, jnp.concatenate([piece, other]), jnp.concatenate([other, piece])
    )


STAGES = (("yh", "yl"), ("x", "z"))


def reduce_grads(grad_w, grad_b):
    total = grad_w.size + grad_b.size
    unit = 2 * group_size(sum(STAGES, ())) * 128
    padded = -(-total // unit) * unit
    flat = jnp.concatenate(
        [grad_w.reshape(-1), grad_b, jnp.zeros((padded - total,), jnp.float32)]
    )
    flat = halve_sum(flat, "c")
    for axes in STAGES:
        flat = scatter_sum(flat, axes)
    flat = flat.astype(jnp.bfloat16)
    for axes in reversed(STAGES):
        flat = gather_back(flat, axes)
    flat = double_back(flat, "c").astype(jnp.float32)
    return flat[: grad_w.size].reshape(grad_w.shape), flat[grad_w.size : total]


def local(volume, block_active, weight, bias, cotangent):
    depth = volume.shape[3]
    blocks = block_active.shape[3]
    edge = depth // blocks
    vox_mask = jnp.repeat(block_active, edge, axis=3)[..., None].astype(jnp.float32)
    masked = volume * vox_mask.astype(jnp.bfloat16)
    padded = with_halo(masked, ((("yh", "z"), 1), (("yl", "c"), 2)), 1)
    padded = jnp.pad(padded, ((0, 0), (0, 0), (0, 0), (1, 1), (0, 0)))
    activated, grad_w, grad_b = layer_work(padded, cotangent, vox_mask, weight, bias)
    grad_w, grad_b = reduce_grads(grad_w, grad_b)
    return (activated, grad_w, grad_b)


def solution(mesh):
    dp, sx, sy = (mesh.shape[name] for name in ("dp", "sx", "sy"))
    shape = (dp, 2, sx // 2, sy // 2, 2)
    physical = Mesh(mesh.devices.reshape(shape), ("x", "yh", "z", "yl", "c"))
    tiles = ("x", ("yh", "z"), ("yl", "c"))
    placed = (
        P(*tiles, None, None),
        P(*tiles, None),
        P(),
        P(),
        P(*tiles, None, None),
    )
    return jax.shard_map(
        local,
        mesh=physical,
        in_specs=placed,
        out_specs=(P(*tiles, None, None), P(), P()),
        check_vma=False,
    )
```
